1024 devices in a mesh: box: 32 (over z, x_lo), param: 32 (over y, x_hi, core).
Axes of the slice: x: 8 (x_hi: 2, x_lo: 4; x = x_hi * 4 + x_lo), y: 8, z: 8, core: 2. Of those that a mesh axis runs over, the one named last changes fastest.
Arguments:
- traces: float32 [32, 32, 512, 256], P('box', 'param'), may hold values from -6 to 6
- owners: int32 [32, 32, 512, 1], P('box', 'param'), may hold values from 0 to 31; in each aligned block of 512 rows (0 to 511, 512 to 1023, ..., all dimensions but the last counted through in order) at most 32 rows name the same one
- counts: int32 [32, 32], P('box', 'param'), may hold values from 128 to 512, as said below
- pair_table: int32 [32, 32, 32, 32], P('box', 'param'), may hold values from 0 to 511
- anterp: float32 [256, 512], replicated, may hold values from -0.375 to 0.375
- interp: float32 [2, 512, 256], replicated, may hold values from -0.25 to 0.25
- phase: float32 [32, 32, 3, 512, 256], P('box', 'param'), may hold values from -3.140625 to 3.140625
Outputs:
- weights_out: float32 [32, 32, 2, 512, 256], P('box', 'param')
The draws below stay inside these ranges and needn't reach their ends.
Inputs may be any that keep to these rules, and one draw needn't show every extreme that they name: `owners`: in the 512 rows of one device no owner is named more than 32 times, a bound that some block reaches. `counts`: some device has all 512 blocks live in every draw.
All inputs are finite; a program needn't handle non-finite values.
Results may differ from the reference program's by a relative error of at most 0.00011.
Values sent between devices are 32-bit elements; how exact they have to be, the bound alone decides.
No kernel may reach another device: no remote copies, remote signals or barrier semaphores. Data moves between devices by JAX's collectives and lax.ppermute only.
A program may use at most 32 MiB of HBM per device.

```python
import math
import jax
import jax.numpy as jnp
import numpy as np
from jax import lax

K = 256
TRACE = 256
PAIRS_DEV = 512
BLK_DEV = 512
LEVELS = 3
CAP = 32
N_BOX = 32
N_PARAM = 32


def draw_counts(key, part):
    first_key, second_key = jax.random.split(jax.random.fold_in(key, 17))
    values = jax.random.randint(first_key, (N_BOX * N_PARAM,), BLK_DEV // 4, BLK_DEV + 1)
    chosen = jax.random.randint(second_key, (), 0, N_BOX * N_PARAM)
    values = jnp.where(jnp.arange(N_BOX * N_PARAM) == chosen, BLK_DEV, values)
    return values.reshape(N_BOX, N_PARAM).astype(jnp.int32)


def set_ends(values, rng, smallest, high):
    dims = values.shape
    index_at = [jax.random.randint(jax.random.fold_in(rng, axis), (), 0, dims[axis]) for axis in range(len(dims))]
    values = values.at[tuple(index_at)].set(smallest)
    longest = dims.index(max(dims))
    index_at[longest] = (index_at[longest] + 1) % dims[longest]
    return values.at[tuple(index_at)].set(high)


def shard_levels(stream_key, shape, cuts, smallest, top_value):
    loudness = 1.0
    for position, parts in cuts:
        draws = jax.random.uniform(jax.random.fold_in(jax.random.fold_in(stream_key, 6), position), (parts,), jnp.float32, smallest / len(cuts), top_value / len(cuts))
        loudness = loudness * jnp.repeat(jnp.exp(draws), shape[position] // parts).reshape((-1,) + (1,) * (len(shape) - 1 - position))
    return loudness


def shared_out(stream_key, own, number, rows, amount, top, limit, slope):
    order = jax.random.permutation(stream_key, amount)
    heavy_load, ordinary = portions_of(amount, rows * top, limit, slope, True), portions_of(amount, rows * top, limit, slope, False)
    places = jnp.arange(amount)

    def named(sizes, turn):
        used = int((sizes > 0).sum())
        fixed = max(1, used // 4)
        passed = fixed + (places - fixed + turn * (used - fixed)) % max(1, amount - fixed)
        return jnp.zeros((amount,), jnp.int32).at[order[jnp.where(places < fixed, places, passed)]].set(jnp.asarray(sizes, jnp.int32))

    sizes = jnp.where(number % 4 == 0, named(heavy_load, number // 4), named(ordinary, number - number // 4 - 1))
    mixed = jax.random.permutation(jax.random.fold_in(own, 3), amount)
    giver, receiver = mixed[0:amount // 2 * 2:2], mixed[1:amount // 2 * 2:2]
    margin = jnp.minimum(sizes[giver] - 1, limit - sizes[receiver]) // 2
    margin = jnp.where((giver == order[0]) | (receiver == order[0]) | (sizes[receiver] == 0), 0, jnp.maximum(margin, 0))
    passed = jax.random.randint(jax.random.fold_in(own, 4), (amount // 2,), 0, 1 << 20) % (margin + 1)
    sizes = sizes.at[giver].add(-passed).at[receiver].add(passed)
    items = jnp.searchsorted(jnp.cumsum(sizes), jnp.arange(rows * top), side="right").astype(jnp.int32)
    listing = items.reshape(top, rows).T
    listing = listing[jax.random.permutation(jax.random.fold_in(own, 1), rows)]
    turn = jax.random.randint(jax.random.fold_in(own, 2), (rows, 1), 0, top)
    return jnp.take_along_axis(listing, (jnp.arange(top)[None, :] + turn) % top, axis=1)


def portions_of(number_of, total, limit, slope, full):
    loads = [(1 << 20) // math.isqrt(rank ** slope) + 1 for rank in range(1, number_of + 1)]
    largest = limit if full else min(limit, max(-(-total // number_of), total * loads[0] // sum(loads)))
    least = 1 if total - largest >= number_of - 1 else 0
    holding, rest = [largest] + [least] * (number_of - 1), total - largest - least * (number_of - 1)
    while rest > 0:
        movable = [i for i in range(1, number_of) if holding[i] < largest] or [i for i in range(1, number_of) if holding[i] < limit]
        whole, budget = sum([loads[i] for i in movable]), rest
        for i in movable:
            more = min(limit - holding[i], max(1, budget * loads[i] // whole), rest)
            holding[i] = holding[i] + more
            rest = rest - more
    return np.array(holding)


def gaussian(key, dims, scale, bound, shards=(), kind=jnp.bfloat16):
    array = jax.random.normal(key, dims, jnp.float32) * scale
    if len(shards) > 0:
        array = shard_levels(key, dims, shards, -0.22, 0.18) * array
    return jnp.clip(array, min=-bound, max=bound).astype(kind)


def setup_inputs(seed: int = 0) -> dict:
    key_list = jax.random.split(jax.random.key(seed), 8)
    traces = gaussian(key_list[0], (N_BOX, N_PARAM, BLK_DEV, TRACE), 1.0, 6.0, ((0, 32), (1, 32)), jnp.float32)
    owners_keys = jax.random.split(jax.random.fold_in(key_list[1], 1), N_BOX * N_PARAM * BLK_DEV // BLK_DEV)
    owners_turns = jax.random.permutation(jax.random.fold_in(key_list[1], 3), N_BOX * N_PARAM * BLK_DEV // BLK_DEV)
    owners = jax.vmap(lambda own, number: shared_out(jax.random.fold_in(key_list[1], 2), own, number, BLK_DEV, N_PARAM, 1, CAP, 2))(owners_keys, owners_turns).reshape((N_BOX, N_PARAM, BLK_DEV, 1))
    counts = draw_counts(jax.random.fold_in(key_list[7], 71), 0)
    pair_table = set_ends(jax.random.randint(key_list[3], (N_BOX, N_PARAM, N_PARAM, CAP), 0, PAIRS_DEV), jax.random.fold_in(key_list[3], 1), 0, PAIRS_DEV - 1).astype(jnp.int32)
    anterp = gaussian(key_list[4], (TRACE, 2 * K), TRACE ** -0.5, 0.375, (), jnp.float32)
    interp = gaussian(key_list[5], (2, 2 * K, K), (2 * K) ** -0.5, 0.25, (), jnp.float32)
    phase = jnp.clip(jax.random.uniform(key_list[6], (N_BOX, N_PARAM, LEVELS, PAIRS_DEV, K), jnp.float32, -3.140625, 3.140625), -3.140625, 3.140625)
    return {"traces": traces, "owners": owners, "counts": counts, "pair_table": pair_table, "anterp": anterp, "interp": interp, "phase": phase}


HIGH = lax.Precision.HIGHEST


def rotate(weights_now, angles):
    cosine = jnp.cos(angles)
    sine_part = jnp.sin(angles)
    real_part = weights_now[..., 0, :, :]
    imag_part = weights_now[..., 1, :, :]
    return jnp.stack([real_part * cosine - imag_part * sine_part, real_part * sine_part + imag_part * cosine], axis=-3)


def reference(traces, owners, counts, pair_table, anterp, interp, phase):
    row_ids = jnp.arange(BLK_DEV, dtype=jnp.int32)
    live_mask = (row_ids[None, None, :] < counts[:, :, None]).astype(jnp.float32)
    destination = owners[..., 0]
    onehot = (destination[..., None] == jnp.arange(N_PARAM, dtype=jnp.int32)).astype(jnp.int32)
    ranking = jnp.sum((jnp.cumsum(onehot, axis=2) - onehot) * onehot, axis=-1).astype(jnp.int32)
    box_ids = jnp.arange(N_BOX, dtype=jnp.int32)[:, None, None]
    source_ids = jnp.arange(N_PARAM, dtype=jnp.int32)[None, :, None]
    pair_ids = pair_table[box_ids, destination, source_ids, ranking]
    coefficient = jnp.einsum("bpnt,tk->bpnk", traces * live_mask[..., None], anterp, precision=HIGH)
    target = ((box_ids * N_PARAM + destination) * PAIRS_DEV + pair_ids).astype(jnp.int32)
    summed = jax.ops.segment_sum(coefficient.reshape(-1, 2 * K), target.reshape(-1), num_segments=N_BOX * N_PARAM * PAIRS_DEV)
    summed = summed.reshape(N_BOX, N_PARAM, PAIRS_DEV, 2, K)
    weights_now = jnp.transpose(summed, (0, 1, 3, 2, 4))
    half_rows = PAIRS_DEV // 2
    for level_id in range(LEVELS):
        span_size = 2 ** level_id
        outer_count = N_BOX // (2 * span_size)
        grouped = weights_now.reshape(outer_count, 2, span_size, N_PARAM, 2, 2, half_rows, K)
        side_parts = []
        for side_id in range(2):
            joined = jnp.concatenate([grouped[:, 0, :, :, :, side_id], grouped[:, 1, :, :, :, side_id]], axis=-1)
            combined = jnp.einsum("hlprqk,skj->hlprsqj", joined, interp, precision=HIGH)
            side_parts.append(combined.reshape(outer_count, span_size, N_PARAM, 2, PAIRS_DEV, K))
        weights_now = jnp.stack(side_parts, axis=1).reshape(N_BOX, N_PARAM, 2, PAIRS_DEV, K)
        weights_now = rotate(weights_now, phase[:, :, level_id])
    return weights_now
```

```python
import jax
import jax.numpy as jnp
from jax import lax
from jax.sharding import PartitionSpec as P

LEVELS = 3


HIGH = lax.Precision.HIGHEST


def swapped(x, axis, bit):
    return lax.ppermute(x, axis, [(i, i ^ 1 << bit) for i in range(lax.axis_size(axis))])


def rotate(weights_now, cosine, sine_part):
    real_part = weights_now[0]
    imag_part = weights_now[1]
    return jnp.stack(
        [real_part * cosine - imag_part * sine_part, real_part * sine_part + imag_part * cosine],
        axis=0,
    )


def shards(traces, owners, counts, pair_table, anterp, interp, phase):
    blocks = traces[0, 0]
    destination = owners[0, 0, :, 0]
    live_count = counts[0, 0]
    param_count = lax.axis_size("param")
    slot_count = pair_table.shape[3]
    block_count = blocks.shape[0]
    trace_count = blocks.shape[1]
    weight_count = interp.shape[2]
    pair_count = phase.shape[3]
    live_mask = (jnp.arange(block_count, dtype=jnp.int32) < live_count).astype(jnp.float32)
    onehot = (destination[:, None] == jnp.arange(param_count, dtype=jnp.int32)[None, :]).astype(
        jnp.int32
    )
    ranking = jnp.sum((jnp.cumsum(onehot, axis=0) - onehot) * onehot, axis=1)
    position = destination * slot_count + ranking
    masked = blocks * live_mask[:, None]
    pair_ids = pair_table[0, 0].reshape(-1)
    selector = (jnp.arange(pair_count, dtype=jnp.int32)[:, None] == pair_ids[None, :]).astype(
        jnp.float32
    )
    outgoing = (
        jnp.zeros((param_count * slot_count, trace_count), jnp.float32).at[position].set(masked)
    )
    arrived = lax.all_to_all(
        outgoing.reshape(param_count, slot_count, trace_count),
        "param",
        split_axis=0,
        concat_axis=0,
        tiled=True,
    )
    angles = phase[0, 0]
    cosines, sines = lax.optimization_barrier((jnp.cos(angles), jnp.sin(angles)))
    gathered = jnp.dot(selector, arrived.reshape(-1, trace_count), precision=HIGH)
    weights_now = jnp.einsum(
        "pt,trk->rpk", gathered, anterp.reshape(trace_count, 2, weight_count), precision=HIGH
    )
    half_rows = pair_count // 2
    box_index = lax.axis_index("box")
    for level_id in range(LEVELS):
        side_bit = box_index >> level_id & 1
        kept_rows = lax.dynamic_slice_in_dim(weights_now, side_bit * half_rows, half_rows, 1)
        sent_rows = lax.dynamic_slice_in_dim(weights_now, (1 - side_bit) * half_rows, half_rows, 1)
        partner = swapped(sent_rows, "box", level_id)
        lower_rows = jnp.where(side_bit == 0, kept_rows, partner)
        upper_rows = jnp.where(side_bit == 0, partner, kept_rows)
        joined = jnp.concatenate([lower_rows, upper_rows], axis=2)
        combined = jnp.einsum("rqk,skj->rsqj", joined, interp, precision=HIGH).reshape(
            2, pair_count, weight_count
        )
        weights_now = rotate(combined, cosines[level_id], sines[level_id])
    return weights_now[None, None]


def solution(mesh):
    placed = (
        P("box", "param", None, None),
        P("box", "param", None, None),
        P("box", "param"),
        P("box", "param", None, None),
        P(),
        P(),
        P("box", "param", None, None, None),
    )
    return jax.shard_map(
        shards,
        mesh=mesh,
        in_specs=placed,
        out_specs=P("box", "param", None, None, None),
        check_vma=False,
    )
```

```python
import jax
import jax.numpy as jnp
from jax import lax
from jax.sharding import PartitionSpec as P


LEVELS = 3
CHUNK_ROWS = (48, 72, 80, 56)
CHUNKS = len(CHUNK_ROWS)


HIGH = lax.Precision.HIGHEST


def swapped(x, axis, bit):
    return lax.ppermute(x, axis, [(i, i ^ 1 << bit) for i in range(lax.axis_size(axis))])


def rotate(weights_now, cosine, sine_part):
    real_part = weights_now[0]
    imag_part = weights_now[1]
    return jnp.stack(
        [real_part * cosine - imag_part * sine_part, real_part * sine_part + imag_part * cosine],
        axis=0,
    )


def shards(traces, owners, counts, pair_table, anterp, interp, phase):
    blocks = traces[0, 0]
    destination = owners[0, 0, :, 0]
    live_count = counts[0, 0]
    param_count = lax.axis_size("param")
    slot_count = pair_table.shape[3]
    block_count = blocks.shape[0]
    trace_count = blocks.shape[1]
    weight_count = interp.shape[2]
    pair_count = phase.shape[3]
    live_mask = (jnp.arange(block_count, dtype=jnp.int32) < live_count).astype(jnp.float32)
    onehot = (destination[:, None] == jnp.arange(param_count, dtype=jnp.int32)[None, :]).astype(
        jnp.int32
    )
    ranking = jnp.sum((jnp.cumsum(onehot, axis=0) - onehot) * onehot, axis=1)
    position = destination * slot_count + ranking
    masked = blocks * live_mask[:, None]
    pair_ids = pair_table[0, 0].reshape(-1)
    selector = (jnp.arange(pair_count, dtype=jnp.int32)[:, None] == pair_ids[None, :]).astype(
        jnp.float32
    )
    outgoing = (
        jnp.zeros((param_count * slot_count, trace_count), jnp.float32).at[position].set(masked)
    )
    arrived = lax.all_to_all(
        outgoing.reshape(param_count, slot_count, trace_count),
        "param",
        split_axis=0,
        concat_axis=0,
        tiled=True,
    )
    angles = phase[0, 0]
    arrived, cosines, sines = lax.optimization_barrier((arrived, jnp.cos(angles), jnp.sin(angles)))
    gathered = jnp.dot(selector, arrived.reshape(-1, trace_count), precision=HIGH)
    weights_now = jnp.einsum(
        "pt,trk->rpk", gathered, anterp.reshape(trace_count, 2, weight_count), precision=HIGH
    )
    half_rows = pair_count // 2
    edges = [sum(CHUNK_ROWS[:i]) * half_rows // 256 for i in range(CHUNKS + 1)]
    cosines = cosines.reshape(LEVELS, 2, half_rows, weight_count)
    sines = sines.reshape(LEVELS, 2, half_rows, weight_count)
    weights_now = weights_now.reshape(2, 2, half_rows, weight_count)
    box_index = lax.axis_index("box")
    pieces = [weights_now[:, :, edges[i]:edges[i + 1]] for i in range(CHUNKS)]
    for level_id in range(LEVELS):
        side_bit = box_index >> level_id & 1
        for i in range(CHUNKS):
            piece = pieces[i]
            kept_rows = lax.dynamic_index_in_dim(piece, side_bit, 1, keepdims=False)
            sent_rows = lax.dynamic_index_in_dim(piece, 1 - side_bit, 1, keepdims=False)
            partner = swapped(sent_rows, "box", level_id)
            lower_rows = jnp.where(side_bit == 0, kept_rows, partner)
            upper_rows = jnp.where(side_bit == 0, partner, kept_rows)
            joined = jnp.concatenate([lower_rows, upper_rows], axis=2)
            combined = jnp.einsum("rqk,skj->rsqj", joined, interp, precision=HIGH)
            rows = slice(edges[i], edges[i + 1])
            pieces[i] = rotate(combined, cosines[level_id][:, rows], sines[level_id][:, rows])
    weights_now = jnp.concatenate(pieces, axis=2).reshape(2, pair_count, weight_count)
    return weights_now[None, None]


def solution(mesh):
    placed = (
        P("box", "param", None, None),
        P("box", "param", None, None),
        P("box", "param"),
        P("box", "param", None, None),
        P(),
        P(),
        P("box", "param", None, None, None),
    )
    return jax.shard_map(
        shards,
        mesh=mesh,
        in_specs=placed,
        out_specs=P("box", "param", None, None, None),
        check_vma=False,
    )
```

```python
import jax
import jax.numpy as jnp
from jax import lax
from jax.sharding import PartitionSpec as P


LEVELS = 3
CHUNK_ROWS = (120, 136)
CHUNKS = len(CHUNK_ROWS)


HIGH = lax.Precision.HIGHEST


def swapped(x, axis, bit):
    return lax.ppermute(x, axis, [(i, i ^ 1 << bit) for i in range(lax.axis_size(axis))])


def rotate(weights_now, cosine, sine_part):
    real_part = weights_now[0]
    imag_part = weights_now[1]
    return jnp.stack(
        [real_part * cosine - imag_part * sine_part, real_part * sine_part + imag_part * cosine],
        axis=0,
    )


def shards(traces, owners, counts, pair_table, anterp, interp, phase):
    blocks = traces[0, 0]
    destination = owners[0, 0, :, 0]
    live_count = counts[0, 0]
    param_count = lax.axis_size("param")
    slot_count = pair_table.shape[3]
    block_count = blocks.shape[0]
    trace_count = blocks.shape[1]
    weight_count = interp.shape[2]
    pair_count = phase.shape[3]
    row_ids = jnp.arange(block_count, dtype=jnp.int32)
    live_mask = (row_ids < live_count).astype(jnp.float32)
    onehot = (destination[:, None] == jnp.arange(param_count, dtype=jnp.int32)[None, :]).astype(
        jnp.float32
    )
    earlier = (row_ids[None, :] < row_ids[:, None]).astype(jnp.float32)
    prior = jnp.dot(earlier, onehot, preferred_element_type=jnp.float32)
    ranking = jnp.sum(prior * onehot, axis=1).astype(jnp.int32)
    position = destination * slot_count + ranking
    pair_ids = pair_table[0, 0].reshape(-1)
    selector = (jnp.arange(pair_count, dtype=jnp.int32)[:, None] == pair_ids[None, :]).astype(
        jnp.float32
    )
    slots = jnp.arange(param_count * slot_count, dtype=jnp.int32)
    placement = jnp.where(slots[:, None] == position[None, :], live_mask[None, :], 0.0)
    outgoing = jnp.dot(placement, blocks, precision=HIGH)
    arrived = lax.all_to_all(
        outgoing.reshape(param_count, slot_count, trace_count),
        "param",
        split_axis=0,
        concat_axis=0,
        tiled=True,
    )
    angles = phase[0, 0]
    arrived, cosines, sines = lax.optimization_barrier((arrived, jnp.cos(angles), jnp.sin(angles)))
    gathered = jnp.dot(selector, arrived.reshape(-1, trace_count), precision=HIGH)
    weights_now = jnp.einsum(
        "pt,trk->rpk", gathered, anterp.reshape(trace_count, 2, weight_count), precision=HIGH
    )
    half_rows = pair_count // 2
    edges = [sum(CHUNK_ROWS[:i]) * half_rows // 256 for i in range(CHUNKS + 1)]
    cosines = cosines.reshape(LEVELS, 2, half_rows, weight_count)
    sines = sines.reshape(LEVELS, 2, half_rows, weight_count)
    weights_now = weights_now.reshape(2, 2, half_rows, weight_count)
    box_index = lax.axis_index("box")
    pieces = [weights_now[:, :, edges[i]:edges[i + 1]] for i in range(CHUNKS)]
    for level_id in range(LEVELS):
        side_bit = box_index >> level_id & 1
        for i in range(CHUNKS):
            piece = pieces[i]
            kept_rows = lax.dynamic_index_in_dim(piece, side_bit, 1, keepdims=False)
            sent_rows = lax.dynamic_index_in_dim(piece, 1 - side_bit, 1, keepdims=False)
            partner = swapped(sent_rows, "box", level_id)
            lower_rows = jnp.where(side_bit == 0, kept_rows, partner)
            upper_rows = jnp.where(side_bit == 0, partner, kept_rows)
            joined = jnp.concatenate([lower_rows, upper_rows], axis=2)
            combined = jnp.einsum("rqk,skj->rsqj", joined, interp, precision=HIGH)
            rows = slice(edges[i], edges[i + 1])
            pieces[i] = rotate(combined, cosines[level_id][:, rows], sines[level_id][:, rows])
    weights_now = jnp.concatenate(pieces, axis=2).reshape(2, pair_count, weight_count)
    return weights_now[None, None]


def solution(mesh):
    placed = (
        P("box", "param", None, None),
        P("box", "param", None, None),
        P("box", "param"),
        P("box", "param", None, None),
        P(),
        P(),
        P("box", "param", None, None, None),
    )
    return jax.shard_map(
        shards,
        mesh=mesh,
        in_specs=placed,
        out_specs=P("box", "param", None, None, None),
        check_vma=False,
    )
```

```python
import jax
import jax.numpy as jnp
from jax import lax
from jax.sharding import PartitionSpec as P


LEVELS = 3
CHUNK_ROWS = (120, 136)
CHUNKS = len(CHUNK_ROWS)


HIGH = lax.Precision.HIGHEST


def swapped(x, axis, bit):
    return lax.ppermute(x, axis, [(i, i ^ 1 << bit) for i in range(lax.axis_size(axis))])


def rotate(weights_now, cosine, sine_part):
    real_part = weights_now[0]
    imag_part = weights_now[1]
    return jnp.stack(
        [real_part * cosine - imag_part * sine_part, real_part * sine_part + imag_part * cosine],
        axis=0,
    )


def shards(traces, owners, counts, pair_table, anterp, interp, phase):
    blocks = traces[0, 0]
    destination = owners[0, 0, :, 0]
    live_count = counts[0, 0]
    param_count = lax.axis_size("param")
    slot_count = pair_table.shape[3]
    block_count = blocks.shape[0]
    trace_count = blocks.shape[1]
    weight_count = interp.shape[2]
    pair_count = phase.shape[3]
    row_ids = jnp.arange(block_count, dtype=jnp.int32)
    live_mask = (row_ids < live_count).astype(jnp.float32)
    onehot = (destination[:, None] == jnp.arange(param_count, dtype=jnp.int32)[None, :]).astype(
        jnp.float32
    )
    earlier = (row_ids[None, :] < row_ids[:, None]).astype(jnp.float32)
    prior = jnp.dot(earlier, onehot, preferred_element_type=jnp.float32)
    ranking = jnp.sum(prior * onehot, axis=1).astype(jnp.int32)
    position = destination * slot_count + ranking
    pair_ids = pair_table[0, 0].reshape(-1)
    selector = (jnp.arange(pair_count, dtype=jnp.int32)[:, None] == pair_ids[None, :]).astype(
        jnp.float32
    )
    slots = jnp.arange(param_count * slot_count, dtype=jnp.int32)
    placement = jnp.where(slots[:, None] == position[None, :], live_mask[None, :], 0.0)
    outgoing = jnp.dot(placement, blocks, precision=HIGH)
    arrived = lax.all_to_all(
        outgoing.reshape(param_count, slot_count, trace_count),
        "param",
        split_axis=0,
        concat_axis=0,
        tiled=True,
    )
    angles = phase[0, 0]
    arrived, cosines, sines = lax.optimization_barrier((arrived, jnp.cos(angles), jnp.sin(angles)))
    gathered = jnp.dot(selector, arrived.reshape(-1, trace_count), precision=HIGH)
    weights_now = jnp.einsum(
        "pt,trk->rpk", gathered, anterp.reshape(trace_count, 2, weight_count), precision=HIGH
    )
    half_rows = pair_count // 2
    edges = [sum(CHUNK_ROWS[:i]) * half_rows // 256 for i in range(CHUNKS + 1)]
    cosines = cosines.reshape(LEVELS, 2, half_rows, weight_count)
    sines = sines.reshape(LEVELS, 2, half_rows, weight_count)
    weights_now = weights_now.reshape(2, 2, half_rows, weight_count)
    box_index = lax.axis_index("box")
    bits = [box_index >> level_id & 1 for level_id in range(LEVELS)]
    kept_parts, sent_parts = [], []
    for i in range(CHUNKS):
        piece = weights_now[:, :, edges[i]:edges[i + 1]]
        kept_parts.append(lax.dynamic_index_in_dim(piece, bits[0], 1, keepdims=False))
        sent_parts.append(lax.dynamic_index_in_dim(piece, 1 - bits[0], 1, keepdims=False))
    outputs = [None] * CHUNKS
    for level_id in range(LEVELS):
        side_bit = bits[level_id]
        own_map = lax.dynamic_slice_in_dim(interp, side_bit * half_rows, half_rows, 1)
        partner_map = lax.dynamic_slice_in_dim(interp, (1 - side_bit) * half_rows, half_rows, 1)
        for i in range(CHUNKS):
            partner = swapped(sent_parts[i], "box", level_id)
            own = jnp.einsum("rqk,skj->srqj", kept_parts[i], own_map, precision=HIGH)
            rows = slice(edges[i], edges[i + 1])

            def half(s, own=own, partner=partner, rows=rows):
                mixed = lax.dynamic_index_in_dim(own, s, 0, keepdims=False) + jnp.einsum(
                    "rqk,kj->rqj",
                    partner,
                    lax.dynamic_index_in_dim(partner_map, s, 0, keepdims=False),
                    precision=HIGH,
                )
                cosine = lax.dynamic_index_in_dim(cosines[level_id], s, 0, keepdims=False)[rows]
                sine_part = lax.dynamic_index_in_dim(sines[level_id], s, 0, keepdims=False)[rows]
                return rotate(mixed, cosine, sine_part)

            if level_id + 1 < LEVELS:
                next_bit = bits[level_id + 1]
                sent_parts[i] = half(1 - next_bit)
                kept_parts[i] = half(next_bit)
            else:
                outputs[i] = jnp.stack([half(0), half(1)], axis=1)
    weights_now = jnp.concatenate(outputs, axis=2).reshape(2, pair_count, weight_count)
    return weights_now[None, None]


def solution(mesh):
    placed = (
        P("box", "param", None, None),
        P("box", "param", None, None),
        P("box", "param"),
        P("box", "param", None, None),
        P(),
        P(),
        P("box", "param", None, None, None),
    )
    return jax.shard_map(
        shards,
        mesh=mesh,
        in_specs=placed,
        out_specs=P("box", "param", None, None, None),
        check_vma=False,
    )
```

```python
import jax
import jax.numpy as jnp
from jax import lax
from jax.sharding import PartitionSpec as P


LEVELS = 3
CHUNK_ROWS = (120, 136)
CHUNKS = len(CHUNK_ROWS)


HIGH = lax.Precision.HIGHEST


def swapped(x, axis, bit):
    return lax.ppermute(x, axis, [(i, i ^ 1 << bit) for i in range(lax.axis_size(axis))])


def rotate(weights_now, cosine, sine_part):
    real_part = weights_now[0]
    imag_part = weights_now[1]
    return jnp.stack(
        [real_part * cosine - imag_part * sine_part, real_part * sine_part + imag_part * cosine],
        axis=0,
    )


def shards(traces, owners, counts, pair_table, anterp, interp, phase):
    blocks = traces[0, 0]
    destination = owners[0, 0, :, 0]
    live_count = counts[0, 0]
    param_count = lax.axis_size("param")
    slot_count = pair_table.shape[3]
    block_count = blocks.shape[0]
    trace_count = blocks.shape[1]
    weight_count = interp.shape[2]
    pair_count = phase.shape[3]
    row_ids = jnp.arange(block_count, dtype=jnp.int32)
    live_mask = (row_ids < live_count).astype(jnp.float32)
    onehot = (destination[:, None] == jnp.arange(param_count, dtype=jnp.int32)[None, :]).astype(
        jnp.float32
    )
    earlier = (row_ids[None, :] < row_ids[:, None]).astype(jnp.float32)
    prior = jnp.dot(earlier, onehot, preferred_element_type=jnp.float32)
    ranking = jnp.sum(prior * onehot, axis=1).astype(jnp.int32)
    position = destination * slot_count + ranking
    pair_ids = pair_table[0, 0].reshape(-1)
    selector = (jnp.arange(pair_count, dtype=jnp.int32)[:, None] == pair_ids[None, :]).astype(
        jnp.float32
    )
    slots = jnp.arange(param_count * slot_count, dtype=jnp.int32)
    placement = jnp.where(slots[:, None] == position[None, :], live_mask[None, :], 0.0)
    outgoing = jnp.dot(placement, blocks, precision=HIGH)
    arrived = lax.all_to_all(
        outgoing.reshape(param_count, slot_count, trace_count),
        "param",
        split_axis=0,
        concat_axis=0,
        tiled=True,
    )
    angles = phase[0, 0]
    arrived, cosines, sines = lax.optimization_barrier((arrived, jnp.cos(angles), jnp.sin(angles)))
    half_rows = pair_count // 2
    edges = [sum(CHUNK_ROWS[:i]) * half_rows // 256 for i in range(CHUNKS + 1)]
    cosines = cosines.reshape(LEVELS, 2, half_rows, weight_count)
    sines = sines.reshape(LEVELS, 2, half_rows, weight_count)
    box_index = lax.axis_index("box")
    bits = [box_index >> level_id & 1 for level_id in range(LEVELS)]
    sources = arrived.reshape(-1, trace_count)
    halves = selector.reshape(2, half_rows, -1)
    anterp_parts = anterp.reshape(trace_count, 2, weight_count)

    def initial(c, i):
        chosen = lax.dynamic_index_in_dim(halves, c, 0, keepdims=False)[edges[i]:edges[i + 1]]
        gathered = jnp.dot(chosen, sources, precision=HIGH)
        return jnp.einsum("pt,trk->rpk", gathered, anterp_parts, precision=HIGH)

    sent_parts, kept_parts = [], []
    for i in range(CHUNKS):
        sent_parts.append(initial(1 - bits[0], i))
        kept_parts.append(initial(bits[0], i))
    outputs = [None] * CHUNKS
    for level_id in range(LEVELS):
        side_bit = bits[level_id]
        own_map = lax.dynamic_slice_in_dim(interp, side_bit * half_rows, half_rows, 1)
        partner_map = lax.dynamic_slice_in_dim(interp, (1 - side_bit) * half_rows, half_rows, 1)
        for i in range(CHUNKS):
            partner = swapped(sent_parts[i], "box", level_id)
            own = jnp.einsum("rqk,skj->srqj", kept_parts[i], own_map, precision=HIGH)
            rows = slice(edges[i], edges[i + 1])

            def half(s, own=own, partner=partner, rows=rows):
                mixed = lax.dynamic_index_in_dim(own, s, 0, keepdims=False) + jnp.einsum(
                    "rqk,kj->rqj",
                    partner,
                    lax.dynamic_index_in_dim(partner_map, s, 0, keepdims=False),
                    precision=HIGH,
                )
                cosine = lax.dynamic_index_in_dim(cosines[level_id], s, 0, keepdims=False)[rows]
                sine_part = lax.dynamic_index_in_dim(sines[level_id], s, 0, keepdims=False)[rows]
                return rotate(mixed, cosine, sine_part)

            if level_id + 1 < LEVELS:
                next_bit = bits[level_id + 1]
                sent_parts[i] = half(1 - next_bit)
                kept_parts[i] = half(next_bit)
            else:
                outputs[i] = jnp.stack([half(0), half(1)], axis=1)
    weights_now = jnp.concatenate(outputs, axis=2).reshape(2, pair_count, weight_count)
    return weights_now[None, None]


def solution(mesh):
    placed = (
        P("box", "param", None, None),
        P("box", "param", None, None),
        P("box", "param"),
        P("box", "param", None, None),
        P(),
        P(),
        P("box", "param", None, None, None),
    )
    return jax.shard_map(
        shards,
        mesh=mesh,
        in_specs=placed,
        out_specs=P("box", "param", None, None, None),
        check_vma=False,
    )
```

```python
import jax
import jax.numpy as jnp
from jax import lax
from jax.sharding import PartitionSpec as P


LEVELS = 3
CHUNK_ROWS = (120, 136)
CHUNKS = len(CHUNK_ROWS)


HIGH = lax.Precision.HIGHEST


def swapped(x, axis, bit):
    return lax.ppermute(x, axis, [(i, i ^ 1 << bit) for i in range(lax.axis_size(axis))])


def rotate(weights_now, cosine, sine_part):
    real_part = weights_now[0]
    imag_part = weights_now[1]
    return jnp.stack(
        [real_part * cosine - imag_part * sine_part, real_part * sine_part + imag_part * cosine],
        axis=0,
    )


def shards(traces, owners, counts, pair_table, anterp, interp, phase):
    blocks = traces[0, 0]
    destination = owners[0, 0, :, 0]
    live_count = counts[0, 0]
    param_count = lax.axis_size("param")
    slot_count = pair_table.shape[3]
    block_count = blocks.shape[0]
    trace_count = blocks.shape[1]
    weight_count = interp.shape[2]
    pair_count = phase.shape[3]
    row_ids = jnp.arange(block_count, dtype=jnp.int32)
    live_mask = (row_ids < live_count).astype(jnp.float32)
    onehot = (destination[:, None] == jnp.arange(param_count, dtype=jnp.int32)[None, :]).astype(
        jnp.float32
    )
    earlier = (row_ids[None, :] < row_ids[:, None]).astype(jnp.float32)
    prior = jnp.dot(earlier, onehot, preferred_element_type=jnp.float32)
    ranking = jnp.sum(prior * onehot, axis=1).astype(jnp.int32)
    position = destination * slot_count + ranking
    pair_ids = pair_table[0, 0].reshape(-1)
    selector = (jnp.arange(pair_count, dtype=jnp.int32)[:, None] == pair_ids[None, :]).astype(
        jnp.float32
    )
    slots = jnp.arange(param_count * slot_count, dtype=jnp.int32)
    placement = jnp.where(slots[:, None] == position[None, :], live_mask[None, :], 0.0)
    top = lax.reduce_precision(blocks, exponent_bits=8, mantissa_bits=7)
    rest = blocks - top
    middle = lax.reduce_precision(rest, exponent_bits=8, mantissa_bits=7)
    pieces = jnp.concatenate([top, middle, rest - middle], axis=0).astype(jnp.bfloat16)
    stacked = jnp.concatenate([placement] * 3, axis=1).astype(jnp.bfloat16)
    outgoing = jnp.dot(stacked, pieces, preferred_element_type=jnp.float32)
    arrived = lax.all_to_all(
        outgoing.reshape(param_count, slot_count, trace_count),
        "param",
        split_axis=0,
        concat_axis=0,
        tiled=True,
    )
    angles = phase[0, 0]
    arrived, cosines, sines = lax.optimization_barrier((arrived, jnp.cos(angles), jnp.sin(angles)))
    half_rows = pair_count // 2
    edges = [sum(CHUNK_ROWS[:i]) * half_rows // 256 for i in range(CHUNKS + 1)]
    cosines = cosines.reshape(LEVELS, 2, half_rows, weight_count)
    sines = sines.reshape(LEVELS, 2, half_rows, weight_count)
    box_index = lax.axis_index("box")
    bits = [box_index >> level_id & 1 for level_id in range(LEVELS)]
    sources = arrived.reshape(-1, trace_count)
    halves = selector.reshape(2, half_rows, -1)
    anterp_parts = anterp.reshape(trace_count, 2, weight_count)

    def initial(c, i):
        chosen = lax.dynamic_index_in_dim(halves, c, 0, keepdims=False)[edges[i]:edges[i + 1]]
        gathered = jnp.dot(chosen, sources, precision=HIGH)
        return jnp.einsum("pt,trk->rpk", gathered, anterp_parts, precision=HIGH)

    sent_parts, kept_parts = [], []
    for i in range(CHUNKS):
        sent_parts.append(initial(1 - bits[0], i))
        kept_parts.append(initial(bits[0], i))
    result = jnp.zeros((2, pair_count, weight_count), jnp.float32)
    for level_id in range(LEVELS):
        side_bit = bits[level_id]
        own_map = lax.dynamic_slice_in_dim(interp, side_bit * half_rows, half_rows, 1)
        partner_map = lax.dynamic_slice_in_dim(interp, (1 - side_bit) * half_rows, half_rows, 1)
        for i in range(CHUNKS):
            partner = swapped(sent_parts[i], "box", level_id)
            own = jnp.einsum("rqk,skj->srqj", kept_parts[i], own_map, precision=HIGH)
            rows = slice(edges[i], edges[i + 1])

            def half(s, own=own, partner=partner, rows=rows):
                mixed = lax.dynamic_index_in_dim(own, s, 0, keepdims=False) + jnp.einsum(
                    "rqk,kj->rqj",
                    partner,
                    lax.dynamic_index_in_dim(partner_map, s, 0, keepdims=False),
                    precision=HIGH,
                )
                cosine = lax.dynamic_index_in_dim(cosines[level_id], s, 0, keepdims=False)[rows]
                sine_part = lax.dynamic_index_in_dim(sines[level_id], s, 0, keepdims=False)[rows]
                return rotate(mixed, cosine, sine_part)

            if level_id + 1 < LEVELS:
                next_bit = bits[level_id + 1]
                sent_parts[i] = half(1 - next_bit)
                kept_parts[i] = half(next_bit)
            else:
                for s in range(2):
                    result = result.at[:, s * half_rows + edges[i]:s * half_rows + edges[i + 1]].set(half(s))
    return result[None, None]


def solution(mesh):
    placed = (
        P("box", "param", None, None),
        P("box", "param", None, None),
        P("box", "param"),
        P("box", "param", None, None),
        P(),
        P(),
        P("box", "param", None, None, None),
    )
    return jax.shard_map(
        shards,
        mesh=mesh,
        in_specs=placed,
        out_specs=P("box", "param", None, None, None),
        check_vma=False,
    )
```

```python
import jax
import jax.numpy as jnp
from jax import lax
from jax.sharding import PartitionSpec as P


LEVELS = 3
CHUNK_ROWS = (144, 112)
CHUNKS = len(CHUNK_ROWS)


HIGH = lax.Precision.HIGHEST


def swapped(x, axis, bit):
    return lax.ppermute(x, axis, [(i, i ^ 1 << bit) for i in range(lax.axis_size(axis))])


def rotate(weights_now, cosine, sine_part):
    real_part = weights_now[0]
    imag_part = weights_now[1]
    return jnp.stack(
        [real_part * cosine - imag_part * sine_part, real_part * sine_part + imag_part * cosine],
        axis=0,
    )


def shards(traces, owners, counts, pair_table, anterp, interp, phase):
    blocks = traces[0, 0]
    destination = owners[0, 0, :, 0]
    live_count = counts[0, 0]
    param_count = lax.axis_size("param")
    slot_count = pair_table.shape[3]
    block_count = blocks.shape[0]
    trace_count = blocks.shape[1]
    weight_count = interp.shape[2]
    pair_count = phase.shape[3]
    row_ids = jnp.arange(block_count, dtype=jnp.int32)
    live_mask = (row_ids < live_count).astype(jnp.float32)
    onehot = (destination[:, None] == jnp.arange(param_count, dtype=jnp.int32)[None, :]).astype(
        jnp.float32
    )
    earlier = (row_ids[None, :] < row_ids[:, None]).astype(jnp.float32)
    prior = jnp.dot(earlier, onehot, preferred_element_type=jnp.float32)
    ranking = jnp.sum(prior * onehot, axis=1).astype(jnp.int32)
    position = destination * slot_count + ranking
    pair_ids = pair_table[0, 0].reshape(-1)
    selector = (jnp.arange(pair_count, dtype=jnp.int32)[:, None] == pair_ids[None, :]).astype(
        jnp.float32
    )
    slots = jnp.arange(param_count * slot_count, dtype=jnp.int32)
    placement = jnp.where(slots[:, None] == position[None, :], live_mask[None, :], 0.0)
    top = lax.reduce_precision(blocks, exponent_bits=8, mantissa_bits=7)
    rest = blocks - top
    middle = lax.reduce_precision(rest, exponent_bits=8, mantissa_bits=7)
    pieces = jnp.concatenate([top, middle, rest - middle], axis=0).astype(jnp.bfloat16)
    stacked = jnp.concatenate([placement] * 3, axis=1).astype(jnp.bfloat16)
    outgoing = jnp.dot(stacked, pieces, preferred_element_type=jnp.float32)
    arrived = lax.all_to_all(
        outgoing.reshape(param_count, slot_count, trace_count),
        "param",
        split_axis=0,
        concat_axis=0,
        tiled=True,
    )
    angles = phase[0, 0]
    arrived, cosines, sines = lax.optimization_barrier((arrived, jnp.cos(angles), jnp.sin(angles)))
    half_rows = pair_count // 2
    edges = [sum(CHUNK_ROWS[:i]) * half_rows // 256 for i in range(CHUNKS + 1)]
    cosines = cosines.reshape(LEVELS, 2, half_rows, weight_count)
    sines = sines.reshape(LEVELS, 2, half_rows, weight_count)
    box_index = lax.axis_index("box")
    bits = [box_index >> level_id & 1 for level_id in range(LEVELS)]
    sources = arrived.reshape(-1, trace_count)
    halves = selector.reshape(2, half_rows, -1)
    anterp_parts = anterp.reshape(trace_count, 2, weight_count)

    def initial(c, i):
        chosen = lax.dynamic_index_in_dim(halves, c, 0, keepdims=False)[edges[i]:edges[i + 1]]
        gathered = jnp.dot(chosen, sources, precision=HIGH)
        return jnp.einsum("pt,trk->rpk", gathered, anterp_parts, precision=HIGH)

    sent_parts, kept_parts = [], []
    for i in range(CHUNKS):
        sent_parts.append(initial(1 - bits[0], i))
        kept_parts.append(initial(bits[0], i))
    outputs = [None] * CHUNKS
    for level_id in range(LEVELS):
        side_bit = bits[level_id]
        own_map = lax.dynamic_slice_in_dim(interp, side_bit * half_rows, half_rows, 1)
        partner_map = lax.dynamic_slice_in_dim(interp, (1 - side_bit) * half_rows, half_rows, 1)
        for i in range(CHUNKS):
            partner = swapped(sent_parts[i], "box", level_id)
            own = jnp.einsum("rqk,skj->srqj", kept_parts[i], own_map, precision=HIGH)
            rows = slice(edges[i], edges[i + 1])

            def half(s, own=own, partner=partner, rows=rows):
                mixed = lax.dynamic_index_in_dim(own, s, 0, keepdims=False) + jnp.einsum(
                    "rqk,kj->rqj",
                    partner,
                    lax.dynamic_index_in_dim(partner_map, s, 0, keepdims=False),
                    precision=HIGH,
                )
                cosine = lax.dynamic_index_in_dim(cosines[level_id], s, 0, keepdims=False)[rows]
                sine_part = lax.dynamic_index_in_dim(sines[level_id], s, 0, keepdims=False)[rows]
                return rotate(mixed, cosine, sine_part)

            if level_id + 1 < LEVELS:
                next_bit = bits[level_id + 1]
                sent_parts[i] = half(1 - next_bit)
                kept_parts[i] = half(next_bit)
            else:
                outputs[i] = jnp.stack([half(0), half(1)], axis=1)
    weights_now = jnp.concatenate(outputs, axis=2).reshape(2, pair_count, weight_count)
    return weights_now[None, None]


def solution(mesh):
    placed = (
        P("box", "param", None, None),
        P("box", "param", None, None),
        P("box", "param"),
        P("box", "param", None, None),
        P(),
        P(),
        P("box", "param", None, None, None),
    )
    return jax.shard_map(
        shards,
        mesh=mesh,
        in_specs=placed,
        out_specs=P("box", "param", None, None, None),
        check_vma=False,
    )
```
